512 devices in a mesh: dp: 4 (over z_lo, core), ctx: 128 (over x, y, z_hi).
Axes of the slice: x: 4, y: 8, z: 8 (z_hi: 4, z_lo: 2; z = z_hi * 2 + z_lo), core: 2. Of those that a mesh axis runs over, the one named last changes fastest.
Arguments:
- query: bfloat16 [4, 32768, 1024], P('dp', 'ctx'), may hold values from -150 to 150
- key: bfloat16 [4, 32768, 1024], P('dp', 'ctx'), may hold values from -3 to 3
- value: bfloat16 [4, 32768, 1024], P('dp', 'ctx'), may hold values from -6 to 6
- grad_out: bfloat16 [4, 32768, 1024], P('dp', 'ctx'), may hold values from -30 to 30
- clause: int32 [4, 32768], P('dp', 'ctx'), may hold values from 0 to 2047, never falling along the last dimension, each value on 1 to 48 neighbouring positions
- bias_table: float32 [32, 2], replicated, may hold values from -1.5 to 1.5
Outputs:
- attended: bfloat16 [4, 32768, 1024], P('dp', 'ctx')
- query_gradient: bfloat16 [4, 32768, 1024], P('dp', 'ctx')
- key_gradient: bfloat16 [4, 32768, 1024], P('dp', 'ctx')
- value_gradient: bfloat16 [4, 32768, 1024], P('dp', 'ctx')
- bias_grad: float32 [32, 2], replicated
The draws below stay inside these ranges and needn't reach their ends.
Inputs may be any that keep to these rules, and one draw needn't show every extreme that they name: Clause ids never fall along a document; a clause holds 1 to 48 tokens, and some clause holds exactly 48.
All inputs are finite; a program needn't handle non-finite values.
Results may differ from the reference program's by a relative error of at most 0.009.
Values may be sent and summed in bfloat16 or wider, within the bound.
No kernel may reach another device: no remote copies, remote signals or barrier semaphores. Data moves between devices by JAX's collectives and lax.ppermute only.
A program may use at most 128 MiB of HBM per device.

```python
import math
import jax
import jax.numpy as jnp
import numpy as np
from jax import lax

ROWS = 256
HEADS = 8
HEAD_DIM = 128
WINDOW = 512
BUCKETS = 32
DILATION_FIRST = 1
DILATION_SECOND = 8
DILATION_THIRD = 32
DOCS = 4
LENGTH = 32768
SEGMENT_FIRST = 4
SEGMENT_SECOND = 32
SEGMENT_THIRD = 128
CLAUSES = 2048


def draw_key(key, part):
    shape = (DOCS, LENGTH, HEADS * HEAD_DIM)
    field = jnp.clip(jax.random.normal(jax.random.fold_in(key, 202), shape), -3.0, 3.0)
    return field.astype(jnp.bfloat16)


def draw_query(key, part):
    shape = (DOCS, LENGTH, HEADS * HEAD_DIM)
    values = jnp.clip(jax.random.normal(jax.random.fold_in(key, 404), shape), -4.0, 4.0)
    return values.astype(jnp.bfloat16)


def draw_grad_out(key, part):
    shape = (DOCS, LENGTH, HEADS * HEAD_DIM)
    base = jax.random.fold_in(key, 505)
    position = jnp.arange(LENGTH).astype(jnp.float32) / LENGTH
    rise = 3.0 ** position
    field = jnp.clip(jax.random.normal(jax.random.fold_in(base, 3), shape), -4.0, 4.0)
    return (field * rise[None, :, None]).astype(jnp.bfloat16)


def block_scale(key, shape, split, smallest, largest):
    def one(dim, blocks):
        draws = jax.random.uniform(jax.random.fold_in(jax.random.fold_in(key, 6), dim), (blocks,), jnp.float32, smallest / len(split), largest / len(split))
        return jnp.repeat(jnp.exp(draws), shape[dim] // blocks).reshape((-1,) + (1,) * (len(shape) - dim - 1))

    level = one(*split[0])
    for cut in split[1:]:
        level = level * one(*cut)
    return level


def profile(count, total, reach, slope):
    weights = [(1 << 20) // math.isqrt(grade ** slope) + 1 for grade in range(2, count + 1)]
    surplus, counts = total - reach - (count - 1), [1] * (count - 1)
    while surplus > 0:
        free = [i for i in range(count - 1) if counts[i] < reach]
        whole, left = sum([weights[i] for i in free]), surplus
        for i in free:
            addition = min(reach - counts[i], max(1, left * weights[i] // whole), surplus)
            counts[i] = counts[i] + addition
            surplus = surplus - addition
    return np.array([reach] + counts)


def ragged(key, number_of, total, limit, skew):
    if number_of == 2:
        one = jax.random.randint(key, (), max(1, total - limit), min(limit, total - 1) + 1)
        return jnp.stack([one, total - one])
    tallies = jnp.asarray(profile(number_of, total, limit, skew), jnp.int32)
    pairs = (number_of - 1) // 2
    donor, taker = tallies[1:1 + 2 * pairs:2], tallies[2:2 + 2 * pairs:2]
    margin = jnp.minimum(donor - 1, limit - taker)
    moved = jax.random.randint(jax.random.fold_in(key, 1), (pairs,), 0, 1 << 20) % (margin + 1)
    tallies = tallies.at[1:1 + 2 * pairs:2].set(donor - moved).at[2:2 + 2 * pairs:2].set(taker + moved)
    return tallies[jax.random.permutation(jax.random.fold_in(key, 2), number_of)]


def noise(rng, shape, spread, most, split=(), kind=jnp.bfloat16):
    entries = jax.random.normal(rng, shape, jnp.float32) * spread
    if len(split) > 0:
        entries = block_scale(rng, shape, split, -0.22, 0.18) * entries
    return jnp.clip(entries, min=-most, max=most).astype(kind)


def setup_inputs(seed: int = 0) -> dict:
    keys = jax.random.split(jax.random.key(seed), 7)
    query = draw_query(jax.random.fold_in(keys[6], 71), 0)
    key = draw_key(jax.random.fold_in(keys[6], 71), 0)
    value = noise(keys[2], (DOCS, LENGTH, HEADS * HEAD_DIM), 1.0, 6.0, ((0, 4), (1, 128)))
    grad_out = draw_grad_out(jax.random.fold_in(keys[6], 71), 0)
    clause = jax.vmap(lambda own: jnp.searchsorted(jnp.cumsum(ragged(own, CLAUSES, LENGTH, 48, 2)), jnp.arange(LENGTH), side="right"))(jax.random.split(keys[4], DOCS)).reshape((DOCS, LENGTH)).astype(jnp.int32)
    bias_table = jnp.clip(jax.random.uniform(keys[5], (BUCKETS, 2), jnp.float32, -1.5, 1.5), -1.5, 1.5)
    return {"query": query, "key": key, "value": value, "grad_out": grad_out, "clause": clause, "bias_table": bias_table}


def sample_rows(matrix, initial_flag, dilation_rate):
    count = matrix.shape[0] // dilation_rate
    head_dim = matrix.shape[1] // HEADS
    grid = matrix.reshape(count, dilation_rate, HEADS, head_dim)
    return jnp.stack([grid[:, 0, initial_flag], grid[:, dilation_rate // 2, initial_flag + 1]], axis=1)


def spread_rows(sampled, dilation_rate):
    count = sampled.shape[0]
    grid = jnp.zeros((count, dilation_rate) + sampled.shape[1:], sampled.dtype)
    grid = grid.at[:, 0, 0].set(sampled[:, 0]).at[:, dilation_rate // 2, 1].set(sampled[:, 1])
    return grid.reshape((count * dilation_rate,) + sampled.shape[1:])


def attend(score_matrix, query_matrix, incoming_keys, incoming_values, gradient_list, score_scale):
    top = jnp.max(score_matrix, axis=-1, keepdims=True)
    raised = jnp.exp(score_matrix - top)
    shares = raised / jnp.sum(raised, axis=-1, keepdims=True)
    softmax_weights = lax.optimization_barrier(shares.astype(jnp.bfloat16)).astype(jnp.float32)
    attended = jnp.einsum("ezb,beo->zeo", softmax_weights, incoming_values.astype(jnp.float32))
    weight_gradient = jnp.einsum("wvx,yvx->vwy", gradient_list.astype(jnp.float32), incoming_values.astype(jnp.float32))
    delta = jnp.sum(shares * weight_gradient, axis=-1, keepdims=True)
    logit_grads = shares * (weight_gradient - delta)
    score_gradient = lax.optimization_barrier(logit_grads.astype(jnp.bfloat16)).astype(jnp.float32)
    query_gradient = jnp.einsum("ezb,beo->zeo", score_gradient, incoming_keys.astype(jnp.float32)) * score_scale
    key_gradient = jnp.einsum("vjb,jvw->bvw", score_gradient, query_matrix.astype(jnp.float32)) * score_scale
    value_gradient = jnp.einsum("vjb,jvw->bvw", softmax_weights, gradient_list.astype(jnp.float32))
    return attended, query_gradient, key_gradient, value_gradient, logit_grads


def band_doc(query, key, value, grad_out, clause, table, score_scale):
    half = WINDOW // 2
    length = query.shape[0]
    head_dim = query.shape[1] // HEADS

    def heads(matrix):
        return matrix[:, :2 * head_dim].reshape(length, 2, head_dim)

    query_matrix, incoming_keys, incoming_values, gradient_list = heads(query), heads(key), heads(value), heads(grad_out)
    padded_keys = jnp.pad(incoming_keys, ((half, half), (0, 0), (0, 0)))
    padded_values = jnp.pad(incoming_values, ((half, half), (0, 0), (0, 0)))
    padded_clause = jnp.pad(clause, (half, half))

    def step(carry, block):
        key_running, value_running, bias_running = carry
        start = block * half
        query_block_rows = lax.dynamic_slice_in_dim(query_matrix, start, half, 0)
        block_grad = lax.dynamic_slice_in_dim(gradient_list, start, half, 0)
        block_clause = lax.dynamic_slice_in_dim(clause, start, half, 0)
        adjacent_keys = lax.dynamic_slice_in_dim(padded_keys, start, 3 * half, 0)
        near_values = lax.dynamic_slice_in_dim(padded_values, start, 3 * half, 0)
        near_clause = lax.dynamic_slice_in_dim(padded_clause, start, 3 * half, 0)
        query_pos = start + jnp.arange(half, dtype=jnp.int32)
        key_pos = start - half + jnp.arange(3 * half, dtype=jnp.int32)
        allowed = (jnp.abs(query_pos[:, None] - key_pos[None, :]) < half) & (key_pos[None, :] >= 0) & (key_pos[None, :] < length)
        bucket = jnp.minimum(jnp.abs(block_clause[:, None] - near_clause[None, :]), BUCKETS - 1)
        score_matrix = jnp.einsum("wvx,yvx->vwy", query_block_rows.astype(jnp.float32), adjacent_keys.astype(jnp.float32)) * score_scale
        score_matrix = score_matrix + jnp.moveaxis(table[bucket], -1, 0)
        score_matrix = jnp.where(allowed[None], score_matrix, -jnp.inf)
        attended, query_gradient, key_gradient, value_gradient, logit_grads = attend(score_matrix, query_block_rows, adjacent_keys, near_values, block_grad, score_scale)
        key_running = lax.dynamic_update_slice_in_dim(key_running, lax.dynamic_slice_in_dim(key_running, start, 3 * half, 0) + key_gradient, start, 0)
        value_running = lax.dynamic_update_slice_in_dim(value_running, lax.dynamic_slice_in_dim(value_running, start, 3 * half, 0) + value_gradient, start, 0)
        bias_running = bias_running + jax.ops.segment_sum(jnp.moveaxis(logit_grads, 0, -1).reshape(-1, 2), bucket.reshape(-1), num_segments=BUCKETS)
        return (key_running, value_running, bias_running), (attended, query_gradient)

    start_state = (jnp.zeros((length + 2 * half, 2, head_dim), jnp.float32), jnp.zeros((length + 2 * half, 2, head_dim), jnp.float32), jnp.zeros((BUCKETS, 2), jnp.float32))
    final, stacked = lax.scan(step, start_state, jnp.arange(length // half, dtype=jnp.int32))
    attended = stacked[0].reshape(length, 2, head_dim)
    query_gradient = stacked[1].reshape(length, 2, head_dim)
    return attended, query_gradient, final[0][half:half + length], final[1][half:half + length], final[2]


def dilated_doc(query, key, value, grad_out, initial_flag, dilation_rate, segment_width, score_scale):
    picked = [sample_rows(matrix, initial_flag, dilation_rate) for matrix in (query, key, value, grad_out)]
    count = picked[0].shape[0]
    per_segment = segment_width * ROWS // dilation_rate
    segments = count // per_segment
    grouped = tuple(matrix.reshape((segments, per_segment) + matrix.shape[1:]) for matrix in picked)

    def one(arrays):
        query_matrix, incoming_keys, incoming_values, gradient_list = arrays
        score_matrix = jnp.einsum("wvx,yvx->vwy", query_matrix.astype(jnp.float32), incoming_keys.astype(jnp.float32)) * score_scale
        result = attend(score_matrix, query_matrix, incoming_keys, incoming_values, gradient_list, score_scale)
        return result[0], result[1], result[2], result[3]

    results = lax.map(one, grouped)
    return [spread_rows(matrix.reshape((count,) + matrix.shape[2:]), dilation_rate) for matrix in results]


def reference(query, key, value, grad_out, clause, bias_table):
    score_scale = HEAD_DIM ** -0.5

    def document(arrays):
        doc_query, doc_key, doc_value, doc_grad, doc_clause = arrays
        band = band_doc(doc_query, doc_key, doc_value, doc_grad, doc_clause, bias_table, score_scale)
        pieces = [band[:4]]
        for initial_flag, dilation_rate, segment_width in ((2, DILATION_FIRST, SEGMENT_FIRST), (4, DILATION_SECOND, SEGMENT_SECOND), (6, DILATION_THIRD, SEGMENT_THIRD)):
            pieces.append(dilated_doc(doc_query, doc_key, doc_value, doc_grad, initial_flag, dilation_rate, segment_width, score_scale))
        length = doc_query.shape[0]
        joined = [jnp.concatenate([piece[slot] for piece in pieces], axis=1).reshape(length, -1).astype(jnp.bfloat16) for slot in range(4)]
        return joined[0], joined[1], joined[2], joined[3], band[4]

    outs = lax.map(document, (query, key, value, grad_out, clause))
    return outs[0], outs[1], outs[2], outs[3], jnp.sum(outs[4], axis=0)
```

```python
import jax
import jax.numpy as jnp
from jax import lax
from jax.sharding import Mesh, PartitionSpec as P

HEADS = 8
WINDOW = 512
BUCKETS = 32
DILATION_FIRST = 1
DILATION_SECOND = 8
DILATION_THIRD = 32
CTX = ("cx", "cy", "cz")


def swapped(block, axis, bit):
    count = lax.axis_size(axis)
    route = []
    for low in range(count):
        high = low | 1 << bit
        if high != low and high < count:
            route += [(low, high), (high, low)]
    return lax.ppermute(block, axis, route)


def shifted(value, axis, steps):
    count = lax.axis_size(axis)
    leading, last = (max(0, -steps), min(count, count - steps))
    return lax.ppermute(value, axis, [(source, source + steps) for source in range(leading, last)])


def with_halo(shard, sides, width):
    for axis, dim in sides:
        size, length = (lax.axis_size(axis), shard.shape[dim])
        up = [(i, (i + 1) % size) for i in range(size - 1)]
        down = [(j, i) for i, j in up]
        last = lax.slice_in_dim(shard, length - width, length, axis=dim)
        leading = lax.slice_in_dim(shard, 0, width, axis=dim)
        before = lax.ppermute(last, axis, up)
        after = lax.ppermute(leading, axis, down)
        shard = jnp.concatenate([before, shard, after], axis=dim)
    return shard


def sample_rows(matrix, initial_flag, dilation_rate):
    count = matrix.shape[0] // dilation_rate
    head_dim = matrix.shape[1] // HEADS
    grid = matrix.reshape(count, dilation_rate, HEADS, head_dim)
    return jnp.concatenate(
        [grid[:, 0, initial_flag], grid[:, dilation_rate // 2, initial_flag + 1]], axis=1
    )


def spread_rows(sampled, dilation_rate):
    count = sampled.shape[0]
    grid = jnp.zeros((count, dilation_rate) + sampled.shape[1:], sampled.dtype)
    grid = grid.at[:, 0, 0].set(sampled[:, 0]).at[:, dilation_rate // 2, 1].set(sampled[:, 1])
    return grid.reshape((count * dilation_rate,) + sampled.shape[1:])


def upper_half(bit):
    index = lax.axis_index(CTX)
    return index // 2**bit % 2 == 1


def double_rows(block, bits):
    for bit in range(bits):
        other = swapped(block, CTX, bit)
        block = jnp.where(
            upper_half(bit),
            jnp.concatenate([other, block], axis=0),
            jnp.concatenate([block, other], axis=0),
        )
    return block


def halve_sums(block, bits):
    for bit in reversed(range(bits)):
        half = block.shape[0] // 2
        lower, higher = (block[:half], block[half:])
        upper = upper_half(bit)
        outgoing = jnp.where(upper, lower, higher)
        staying = jnp.where(upper, higher, lower)
        block = staying + swapped(outgoing.astype(jnp.bfloat16), CTX, bit).astype(outgoing.dtype)
    return block


def span_rows(block, bits):
    return double_rows(block, bits)


def span_sums(block, bits):
    return halve_sums(block, bits)


def rows_side(score_matrix, every_key_rows, every_value_rows, gradient_list, score_scale):
    top = jnp.max(score_matrix, axis=-1, keepdims=True)
    raised = jnp.exp(score_matrix - top)
    totals = jnp.sum(raised, axis=-1, keepdims=True)
    shares = raised / totals
    softmax_weights = shares.astype(jnp.bfloat16)
    attended = jnp.einsum(
        "ezb,beo->zeo", softmax_weights, every_value_rows, preferred_element_type=jnp.float32
    )
    weight_gradient = jnp.einsum(
        "wvx,yvx->vwy", gradient_list, every_value_rows, preferred_element_type=jnp.float32
    )
    delta = jnp.sum(shares * weight_gradient, axis=-1, keepdims=True)
    logit_grads = shares * (weight_gradient - delta)
    score_gradient = logit_grads.astype(jnp.bfloat16)
    query_gradient = (
        jnp.einsum(
            "ezb,beo->zeo", score_gradient, every_key_rows, preferred_element_type=jnp.float32
        )
        * score_scale
    )
    return (
        attended,
        query_gradient,
        softmax_weights,
        score_gradient,
        logit_grads,
        top,
        totals,
        delta,
    )


def keys_side(softmax_weights, score_gradient, query_matrix, gradient_list, score_scale):
    key_gradient = (
        jnp.einsum("vjb,jvw->bvw", score_gradient, query_matrix, preferred_element_type=jnp.float32)
        * score_scale
    )
    value_gradient = jnp.einsum(
        "vjb,jvw->bvw", softmax_weights, gradient_list, preferred_element_type=jnp.float32
    )
    return (key_gradient, value_gradient)


def bucket_lookup(bucket, table):
    running = jnp.zeros((table.shape[1],) + bucket.shape, jnp.float32)
    for level in range(BUCKETS):
        running = jnp.where(bucket[None] == level, table[level][:, None, None], running)
    return running


def bucket_sums(bucket, logit_grads):
    totals = [
        jnp.sum(jnp.where(bucket[None] == level, logit_grads, 0.0), axis=(1, 2))
        for level in range(BUCKETS)
    ]
    return jnp.stack(totals, axis=0)


def pass_rim(rim, offset):
    return shifted(rim.astype(jnp.bfloat16), CTX, offset).astype(rim.dtype)


def band_part(query_rows, key_rows, value_rows, grad_rows, clause_rows, table, score_scale):
    rows, width = query_rows.shape
    head_dim = width // HEADS
    wide = 2 * head_dim
    half = WINDOW // 2
    pair_rows = jnp.concatenate([key_rows[:, :wide], value_rows[:, :wide]], axis=1)
    extended, extended_clause = (
        with_halo(pair_rows, ((CTX, 0),), half),
        with_halo(clause_rows, ((CTX, 0),), half),
    )
    reach = rows + 2 * half
    nearby_key_rows = extended[:, :wide].reshape(reach, 2, head_dim)
    values_near = extended[:, wide:].reshape(reach, 2, head_dim)
    query_matrix = query_rows[:, :wide].reshape(rows, 2, head_dim)
    gradient_list = grad_rows[:, :wide].reshape(rows, 2, head_dim)
    start = lax.axis_index(CTX) * rows
    length = rows * lax.axis_size(CTX)
    local_query = jnp.arange(rows)[:, None]
    local_key = jnp.arange(reach)[None, :] - half
    global_key = start + local_key
    allowed = (jnp.abs(local_query - local_key) < half) & (global_key >= 0) & (global_key < length)
    bucket = jnp.minimum(jnp.abs(clause_rows[:, None] - extended_clause[None, :]), BUCKETS - 1)
    score_matrix = (
        jnp.einsum(
            "wvx,yvx->vwy", query_matrix, nearby_key_rows, preferred_element_type=jnp.float32
        )
        * score_scale
    )
    score_matrix = jnp.where(allowed[None], score_matrix + bucket_lookup(bucket, table), -jnp.inf)
    attended, query_gradient, softmax_weights, score_gradient, logit_grads, top, totals, delta = (
        rows_side(score_matrix, nearby_key_rows, values_near, gradient_list, score_scale)
    )
    key_gradient, value_gradient = keys_side(
        softmax_weights, score_gradient, query_matrix, gradient_list, score_scale
    )
    sums = jnp.concatenate(
        [key_gradient.reshape(reach, wide), value_gradient.reshape(reach, wide)], axis=1
    )
    own = sums[half : half + rows]
    from_next = pass_rim(sums[:half], -1)
    from_prev = pass_rim(sums[half + rows :], 1)
    own = own.at[rows - half :].add(from_next).at[:half].add(from_prev)
    own_key = own[:, :wide].reshape(rows, 2, head_dim)
    own_value = own[:, wide:].reshape(rows, 2, head_dim)
    return (attended, query_gradient, own_key, own_value, bucket_sums(bucket, logit_grads))


def dilated(
    query_rows, key_rows, value_rows, grad_rows, initial_flag, dilation_rate, bits, score_scale
):
    head_dim = query_rows.shape[1] // HEADS
    wide = 2 * head_dim
    picked_query = sample_rows(query_rows, initial_flag, dilation_rate)
    picked_key = sample_rows(key_rows, initial_flag, dilation_rate)
    picked_value = sample_rows(value_rows, initial_flag, dilation_rate)
    picked_grad = sample_rows(grad_rows, initial_flag, dilation_rate)
    count = picked_query.shape[0]
    gathered = lax.all_gather(
        jnp.concatenate([picked_key, picked_value], axis=1), bits, axis=0, tiled=True
    )
    gathered_rows = gathered.shape[0]
    every_key_rows = gathered[:, :wide].reshape(gathered_rows, 2, head_dim)
    every_value_rows = gathered[:, wide:].reshape(gathered_rows, 2, head_dim)
    query_matrix = picked_query.reshape(count, 2, head_dim)
    gradient_list = picked_grad.reshape(count, 2, head_dim)
    score_matrix = (
        jnp.einsum("wvx,yvx->vwy", query_matrix, every_key_rows, preferred_element_type=jnp.float32)
        * score_scale
    )
    attended, query_gradient, softmax_weights, score_gradient, logit_grads, top, totals, delta = (
        rows_side(score_matrix, every_key_rows, every_value_rows, gradient_list, score_scale)
    )
    key_gradient, value_gradient = keys_side(
        softmax_weights, score_gradient, query_matrix, gradient_list, score_scale
    )
    partial_sums = jnp.concatenate(
        [key_gradient.reshape(gathered_rows, wide), value_gradient.reshape(gathered_rows, wide)],
        axis=1,
    )
    own = lax.psum_scatter(partial_sums, bits, scatter_dimension=0, tiled=True)
    own_key = own[:, :wide].reshape(count, 2, head_dim)
    own_value = own[:, wide:].reshape(count, 2, head_dim)
    return (
        spread_rows(attended, dilation_rate),
        spread_rows(query_gradient, dilation_rate),
        spread_rows(own_key, dilation_rate),
        spread_rows(own_value, dilation_rate),
    )


def shards(query, key, value, grad_out, clause, bias_table):
    query_rows = query[0]
    key_rows = key[0]
    value_rows = value[0]
    grad_rows = grad_out[0]
    clause_rows = clause[0]
    rows, width = query_rows.shape
    head_dim = width // HEADS
    score_scale = head_dim ** (-0.5)
    band = band_part(
        query_rows, key_rows, value_rows, grad_rows, clause_rows, bias_table, score_scale
    )
    pieces = [band[:4]]
    for initial_flag, dilation_rate, bits in (
        (2, DILATION_FIRST, CTX[2:]),
        (4, DILATION_SECOND, CTX[1:]),
        (6, DILATION_THIRD, CTX),
    ):
        pieces.append(
            dilated(
                query_rows,
                key_rows,
                value_rows,
                grad_rows,
                initial_flag,
                dilation_rate,
                bits,
                score_scale,
            )
        )
    bias_grad = lax.psum(band[4], ("dp",) + CTX)
    joined = [
        jnp.concatenate([piece[slot] for piece in pieces], axis=1)
        .reshape(1, rows, width)
        .astype(jnp.bfloat16)
        for slot in range(4)
    ]
    return (joined[0], joined[1], joined[2], joined[3], bias_grad)


def solution(mesh):
    ctx_size = mesh.shape["ctx"]
    parts = (4, 8, ctx_size // 32)
    split = Mesh(mesh.devices.reshape((mesh.shape["dp"],) + parts), ("dp",) + CTX)
    in_specs = (
        P("dp", CTX, None),
        P("dp", CTX, None),
        P("dp", CTX, None),
        P("dp", CTX, None),
        P("dp", CTX),
        P(),
    )
    out_specs = (
        P("dp", CTX, None),
        P("dp", CTX, None),
        P("dp", CTX, None),
        P("dp", CTX, None),
        P(),
    )
    return jax.shard_map(shards, mesh=split, in_specs=in_specs, out_specs=out_specs, check_vma=False)
```

```python
import jax
import jax.numpy as jnp
from jax import lax
from jax.sharding import Mesh, PartitionSpec as P

HEADS = 8
WINDOW = 512
BUCKETS = 32
DILATION_FIRST = 1
DILATION_SECOND = 8
DILATION_THIRD = 32
CTX = ("cx", "cy", "cz")


def swapped(block, axis, bit):
    count = lax.axis_size(axis)
    route = []
    for low in range(count):
        high = low | 1 << bit
        if high != low and high < count:
            route += [(low, high), (high, low)]
    return lax.ppermute(block, axis, route)


def shifted(value, axis, steps):
    count = lax.axis_size(axis)
    leading, last = (max(0, -steps), min(count, count - steps))
    return lax.ppermute(value, axis, [(source, source + steps) for source in range(leading, last)])


def with_halo(shard, sides, width):
    for axis, dim in sides:
        size, length = (lax.axis_size(axis), shard.shape[dim])
        up = [(i, (i + 1) % size) for i in range(size - 1)]
        down = [(j, i) for i, j in up]
        last = lax.slice_in_dim(shard, length - width, length, axis=dim)
        leading = lax.slice_in_dim(shard, 0, width, axis=dim)
        before = lax.ppermute(last, axis, up)
        after = lax.ppermute(leading, axis, down)
        shard = jnp.concatenate([before, shard, after], axis=dim)
    return shard


def sample_rows(matrix, initial_flag, dilation_rate):
    count = matrix.shape[0] // dilation_rate
    head_dim = matrix.shape[1] // HEADS
    grid = matrix.reshape(count, dilation_rate, HEADS, head_dim)
    return jnp.concatenate(
        [grid[:, 0, initial_flag], grid[:, dilation_rate // 2, initial_flag + 1]], axis=1
    )


def spread_rows(sampled, dilation_rate):
    count = sampled.shape[0]
    grid = jnp.zeros((count, dilation_rate) + sampled.shape[1:], sampled.dtype)
    grid = grid.at[:, 0, 0].set(sampled[:, 0]).at[:, dilation_rate // 2, 1].set(sampled[:, 1])
    return grid.reshape((count * dilation_rate,) + sampled.shape[1:])


def upper_half(bit):
    index = lax.axis_index(CTX)
    return index // 2**bit % 2 == 1


def double_rows(block, bits):
    for bit in range(bits):
        other = swapped(block, CTX, bit)
        block = jnp.where(
            upper_half(bit),
            jnp.concatenate([other, block], axis=0),
            jnp.concatenate([block, other], axis=0),
        )
    return block


def halve_sums(block, bits):
    for bit in reversed(range(bits)):
        half = block.shape[0] // 2
        lower, higher = (block[:half], block[half:])
        upper = upper_half(bit)
        outgoing = jnp.where(upper, lower, higher)
        staying = jnp.where(upper, higher, lower)
        block = staying + swapped(outgoing.astype(jnp.bfloat16), CTX, bit).astype(outgoing.dtype)
    return block


def span_rows(block, bits):
    return double_rows(block, bits)


def span_sums(block, bits):
    return halve_sums(block, bits)


def rows_side(score_matrix, every_key_rows, every_value_rows, gradient_list, score_scale):
    top = jnp.max(score_matrix, axis=-1, keepdims=True)
    raised = jnp.exp(score_matrix - top)
    totals = jnp.sum(raised, axis=-1, keepdims=True)
    shares = raised / totals
    softmax_weights = shares.astype(jnp.bfloat16)
    attended = jnp.einsum(
        "ezb,beo->zeo", softmax_weights, every_value_rows, preferred_element_type=jnp.float32
    )
    weight_gradient = jnp.einsum(
        "wvx,yvx->vwy", gradient_list, every_value_rows, preferred_element_type=jnp.float32
    )
    delta = jnp.sum(shares * weight_gradient, axis=-1, keepdims=True)
    logit_grads = shares * (weight_gradient - delta)
    score_gradient = logit_grads.astype(jnp.bfloat16)
    query_gradient = (
        jnp.einsum(
            "ezb,beo->zeo", score_gradient, every_key_rows, preferred_element_type=jnp.float32
        )
        * score_scale
    )
    return (
        attended,
        query_gradient,
        softmax_weights,
        score_gradient,
        logit_grads,
        top,
        totals,
        delta,
    )


def keys_side(softmax_weights, score_gradient, query_matrix, gradient_list, score_scale):
    key_gradient = (
        jnp.einsum("vjb,jvw->bvw", score_gradient, query_matrix, preferred_element_type=jnp.float32)
        * score_scale
    )
    value_gradient = jnp.einsum(
        "vjb,jvw->bvw", softmax_weights, gradient_list, preferred_element_type=jnp.float32
    )
    return (key_gradient, value_gradient)


def bucket_lookup(bucket, table):
    running = jnp.zeros((table.shape[1],) + bucket.shape, jnp.float32)
    for level in range(BUCKETS):
        running = jnp.where(bucket[None] == level, table[level][:, None, None], running)
    return running


def bucket_sums(bucket, logit_grads):
    totals = [
        jnp.sum(jnp.where(bucket[None] == level, logit_grads, 0.0), axis=(1, 2))
        for level in range(BUCKETS)
    ]
    return jnp.stack(totals, axis=0)


def pass_rim(rim, offset):
    return shifted(rim.astype(jnp.bfloat16), CTX, offset).astype(rim.dtype)


def band_part(query_rows, key_rows, value_rows, grad_rows, clause_rows, table, score_scale):
    rows, width = query_rows.shape
    head_dim = width // HEADS
    wide = 2 * head_dim
    half = WINDOW // 2
    pair_rows = jnp.concatenate([key_rows[:, :wide], value_rows[:, :wide]], axis=1)
    extended, extended_clause = (
        with_halo(pair_rows, ((CTX, 0),), half),
        with_halo(clause_rows, ((CTX, 0),), half),
    )
    reach = rows + 2 * half
    nearby_key_rows = extended[:, :wide].reshape(reach, 2, head_dim)
    values_near = extended[:, wide:].reshape(reach, 2, head_dim)
    query_matrix = query_rows[:, :wide].reshape(rows, 2, head_dim)
    gradient_list = grad_rows[:, :wide].reshape(rows, 2, head_dim)
    start = lax.axis_index(CTX) * rows
    length = rows * lax.axis_size(CTX)
    local_query = jnp.arange(rows)[:, None]
    local_key = jnp.arange(reach)[None, :] - half
    global_key = start + local_key
    allowed = (jnp.abs(local_query - local_key) < half) & (global_key >= 0) & (global_key < length)
    bucket = jnp.minimum(jnp.abs(clause_rows[:, None] - extended_clause[None, :]), BUCKETS - 1)
    score_matrix = (
        jnp.einsum(
            "wvx,yvx->vwy", query_matrix, nearby_key_rows, preferred_element_type=jnp.float32
        )
        * score_scale
    )
    score_matrix = jnp.where(allowed[None], score_matrix + bucket_lookup(bucket, table), -jnp.inf)
    attended, query_gradient, softmax_weights, score_gradient, logit_grads, top, totals, delta = (
        rows_side(score_matrix, nearby_key_rows, values_near, gradient_list, score_scale)
    )
    key_gradient, value_gradient = keys_side(
        softmax_weights, score_gradient, query_matrix, gradient_list, score_scale
    )
    sums = jnp.concatenate(
        [key_gradient.reshape(reach, wide), value_gradient.reshape(reach, wide)], axis=1
    )
    own = sums[half : half + rows]
    from_next = pass_rim(sums[:half], -1)
    from_prev = pass_rim(sums[half + rows :], 1)
    own = own.at[rows - half :].add(from_next).at[:half].add(from_prev)
    own_key = own[:, :wide].reshape(rows, 2, head_dim)
    own_value = own[:, wide:].reshape(rows, 2, head_dim)
    return (attended, query_gradient, own_key, own_value, bucket_sums(bucket, logit_grads))


def dilated_picks(query_rows, key_rows, value_rows, grad_rows, initial_flag, dilation_rate):
    picked = [
        sample_rows(matrix, initial_flag, dilation_rate)
        for matrix in (query_rows, key_rows, value_rows, grad_rows)
    ]
    return picked[0], jnp.concatenate([picked[1], picked[2]], axis=1), picked[3]


def dilated_math(picked_query, gathered, picked_grad, score_scale):
    head_dim = picked_query.shape[1] // 2
    wide = 2 * head_dim
    count = picked_query.shape[0]
    gathered_rows = gathered.shape[0]
    every_key_rows = gathered[:, :wide].reshape(gathered_rows, 2, head_dim)
    every_value_rows = gathered[:, wide:].reshape(gathered_rows, 2, head_dim)
    query_matrix = picked_query.reshape(count, 2, head_dim)
    gradient_list = picked_grad.reshape(count, 2, head_dim)
    score_matrix = (
        jnp.einsum("wvx,yvx->vwy", query_matrix, every_key_rows, preferred_element_type=jnp.float32)
        * score_scale
    )
    attended, query_gradient, softmax_weights, score_gradient, logit_grads, top, totals, delta = (
        rows_side(score_matrix, every_key_rows, every_value_rows, gradient_list, score_scale)
    )
    key_gradient, value_gradient = keys_side(
        softmax_weights, score_gradient, query_matrix, gradient_list, score_scale
    )
    partial_sums = jnp.concatenate(
        [key_gradient.reshape(gathered_rows, wide), value_gradient.reshape(gathered_rows, wide)],
        axis=1,
    )
    return attended, query_gradient, partial_sums


def merged_doubling(blocks, bits):
    for bit in range(max(bits)):
        active = [g for g in range(len(blocks)) if bits[g] > bit]
        payload = jnp.concatenate([blocks[g] for g in active], axis=0)
        other = swapped(payload, CTX, bit)
        offset = 0
        upper = upper_half(bit)
        for g in active:
            size = blocks[g].shape[0]
            piece = other[offset : offset + size]
            offset += size
            blocks[g] = jnp.where(
                upper,
                jnp.concatenate([piece, blocks[g]], axis=0),
                jnp.concatenate([blocks[g], piece], axis=0),
            )
    return blocks


def split_three(total):
    flat = total.reshape(1, -1)
    first = flat.astype(jnp.bfloat16)
    rest = flat - first.astype(jnp.float32)
    second = rest.astype(jnp.bfloat16)
    third = (rest - second.astype(jnp.float32)).astype(jnp.bfloat16)
    return jnp.concatenate([first, second, third], axis=0)


def join_three(pieces, shape):
    parts = pieces.astype(jnp.float32)
    return ((parts[0] + parts[1]) + parts[2]).reshape(shape)


def merged_halving(blocks, bits, bias):
    width = blocks[0].shape[1]
    count = bias.size
    for bit in reversed(range(max(bits))):
        active = [g for g in range(len(blocks)) if bits[g] > bit]
        upper = upper_half(bit)
        staying, outgoing = [], []
        for g in active:
            half = blocks[g].shape[0] // 2
            lower, higher = blocks[g][:half], blocks[g][half:]
            outgoing.append(jnp.where(upper, lower, higher).astype(jnp.bfloat16))
            staying.append(jnp.where(upper, higher, lower))
        coded = jnp.pad(split_three(bias), ((0, 5), (0, width - count)))
        payload = jnp.concatenate(outgoing + [coded], axis=0)
        other = swapped(payload, CTX, bit)
        offset = 0
        for g, stay in zip(active, staying):
            size = stay.shape[0]
            blocks[g] = stay + other[offset : offset + size].astype(stay.dtype)
            offset += size
        bias = bias + join_three(other[offset : offset + 3, :count], bias.shape)
    return blocks, bias


def segment_size(axes):
    size = 1
    for axis in axes:
        size *= lax.axis_size(axis)
    return size


def spread_to_segment(block, axes):
    count = segment_size(axes)
    copies = jnp.broadcast_to(block[None], (count,) + block.shape)
    return lax.all_to_all(copies, axes, 0, 0, tiled=True).reshape((-1, block.shape[1]))


def sum_from_segment(partial_sums, axes, bias):
    count = segment_size(axes)
    width = partial_sums.shape[1]
    chunks = partial_sums.reshape((count, -1, width)).astype(jnp.bfloat16)
    if bias is not None:
        coded = jnp.pad(split_three(bias), ((0, 5), (0, width - bias.size)))
        chunks = jnp.concatenate(
            [chunks, jnp.broadcast_to(coded[None], (count,) + coded.shape)], axis=1
        )
    arrived = lax.all_to_all(chunks, axes, 0, 0, tiled=True).astype(jnp.float32)
    rows = partial_sums.shape[0] // count
    own = jnp.sum(arrived[:, :rows], axis=0)
    if bias is None:
        return own, None
    parts = arrived[:, rows : rows + 3, : bias.size]
    return own, jnp.sum((parts[:, 0] + parts[:, 1]) + parts[:, 2], axis=0).reshape(bias.shape)


def dp_sum(total):
    for bit in range(lax.axis_size("dp").bit_length() - 1):
        total = total + swapped(total, "dp", bit)
    return total


def shards(query, key, value, grad_out, clause, bias_table):
    query_rows = query[0]
    key_rows = key[0]
    value_rows = value[0]
    grad_rows = grad_out[0]
    clause_rows = clause[0]
    rows, width = query_rows.shape
    head_dim = width // HEADS
    score_scale = head_dim ** (-0.5)
    band = band_part(
        query_rows, key_rows, value_rows, grad_rows, clause_rows, bias_table, score_scale
    )
    plans = (
        (2, DILATION_FIRST, CTX[2:]),
        (4, DILATION_SECOND, CTX[1:]),
        (6, DILATION_THIRD, CTX),
    )
    picks = [
        dilated_picks(query_rows, key_rows, value_rows, grad_rows, flag, rate)
        for flag, rate, _ in plans
    ]
    groups = [plan[2] for plan in plans]
    gathered = [spread_to_segment(pick[1], axes) for pick, axes in zip(picks, groups)]
    results = [
        dilated_math(pick[0], block, pick[2], score_scale) for pick, block in zip(picks, gathered)
    ]
    total = dp_sum(band[4])
    sums = []
    for result, axes in zip(results, groups):
        own, total = (
            sum_from_segment(result[2], axes, total) if axes == CTX else (
                sum_from_segment(result[2], axes, None)[0], total
            )
        )
        sums.append(own)
    bias_grad = total
    pieces = [band[:4]]
    for (flag, rate, _), result, own in zip(plans, results, sums):
        count = own.shape[0]
        wide = 2 * head_dim
        pieces.append(
            [
                spread_rows(result[0], rate),
                spread_rows(result[1], rate),
                spread_rows(own[:, :wide].reshape(count, 2, head_dim), rate),
                spread_rows(own[:, wide:].reshape(count, 2, head_dim), rate),
            ]
        )
    joined = [
        jnp.concatenate([piece[slot] for piece in pieces], axis=1)
        .reshape(1, rows, width)
        .astype(jnp.bfloat16)
        for slot in range(4)
    ]
    return (joined[0], joined[1], joined[2], joined[3], bias_grad)


def solution(mesh):
    parts = (4, 8, mesh.shape["ctx"] // 32)
    split = Mesh(mesh.devices.reshape((mesh.shape["dp"],) + parts), ("dp",) + CTX)
    in_specs = (
        P("dp", CTX, None),
        P("dp", CTX, None),
        P("dp", CTX, None),
        P("dp", CTX, None),
        P("dp", CTX),
        P(),
    )
    out_specs = (
        P("dp", CTX, None),
        P("dp", CTX, None),
        P("dp", CTX, None),
        P("dp", CTX, None),
        P(),
    )
    return jax.shard_map(shards, mesh=split, in_specs=in_specs, out_specs=out_specs, check_vma=False)
```
